1024 devices in a mesh: expert: 16 (over x, core), section: 16 (over z, y_lo), dp: 4 (over y_hi).
Axes of the slice: x: 8, y: 8 (y_hi: 4, y_lo: 2; y = y_hi * 2 + y_lo), z: 8, core: 2. Of those that a mesh axis runs over, the one named last changes fastest.
Arguments:
- tok_input: bfloat16 [16, 4, 2048, 2048], P('section', 'dp', 'expert'), may hold values from -6 to 6
- tok_grad: bfloat16 [16, 4, 2048, 2048], P('section', 'dp', 'expert'), may hold values from -6 to 6
- combine_weight: float32 [16, 4, 2048], P('section', 'dp', 'expert'), may hold values from 0.1 to 1
- route_expert: int32 [16, 4, 2048], P('section', 'dp', 'expert'), may hold values from 0 to 7, as said below
- gate_up_weight: bfloat16 [16, 16, 2048, 768], P('section', 'expert'), may hold values from -0.125 to 0.125
- down_weight: bfloat16 [16, 16, 384, 2048], P('section', 'expert'), may hold values from -0.21875 to 0.21875
Outputs:
- gate_up_grad: bfloat16 [16, 16, 2048, 768], P('section', 'expert', 'dp')
- upstream: bfloat16 [16, 4, 2048, 2048], P('section', 'dp', 'expert')
The draws below stay inside these ranges and needn't reach their ends.
Inputs may be any that keep to these rules, and one draw needn't show every extreme that they name: `route_expert`: among the tokens of one device, at most 18 name one expert, and in every such block some expert is named by exactly 18; in some section and data group one expert is named by 18 tokens of every device.
All inputs are finite; a program needn't handle non-finite values.
Results may differ from the reference program's by a relative error of at most 0.013.
Values may be sent and summed in bfloat16 or wider, within the bound.
No kernel may reach another device: no remote copies, remote signals or barrier semaphores. Data moves between devices by JAX's collectives and lax.ppermute only.
A program may use at most 64 MiB of HBM per device.

```python
import jax
import jax.numpy as jnp
from jax import lax

D = 2048
FF = 768
TOK_DEV = 128
FD = 384
EXPERTS = 8
CAP = 18
TOKENS = 2048
N_EXPERT = 16
N_SECTION = 16
N_DP = 4


def block_routes(key, hot_shared, use_shared):
    key_hot, key_shift, key_order, key_tokens = jax.random.split(key, 4)
    hottest = jnp.where(use_shared, hot_shared, jax.random.randint(key_hot, (), 0, EXPERTS, dtype=jnp.int32))
    others = EXPERTS - 1
    remaining = TOK_DEV - CAP
    share = remaining // others
    leftover = remaining % others
    spread = max(0, min(share - 1, CAP - share - 2))
    pair_count = max(1, others // 2)
    amounts = jax.random.randint(key_shift, (pair_count,), -spread, spread + 1, dtype=jnp.int32)
    other_index = jnp.arange(others, dtype=jnp.int32)
    paired = other_index // 2
    in_pair = paired < others // 2
    signs = jnp.where(other_index % 2 == 0, 1, -1).astype(jnp.int32)
    shifts = jnp.where(in_pair, signs * amounts[jnp.minimum(paired, pair_count - 1)], 0)
    counts_other = share + (other_index < leftover).astype(jnp.int32) + shifts
    counts_other = counts_other[jax.random.permutation(key_order, others)]
    where_other = (hottest + 1 + other_index) % EXPERTS
    counts = jnp.zeros((EXPERTS,), jnp.int32).at[where_other].set(counts_other).at[hottest].set(CAP)
    bounds = jnp.cumsum(counts).astype(jnp.int32)
    position = jnp.arange(TOK_DEV, dtype=jnp.int32)
    expert_of = jnp.sum((bounds[None, :] <= position[:, None]).astype(jnp.int32), axis=1)
    return expert_of[jax.random.permutation(key_tokens, TOK_DEV)].astype(jnp.int32)


def draw_route_expert(key, part):
    groups_total = N_SECTION * N_DP
    group_keys = jax.random.split(jax.random.fold_in(key, 7), groups_total)
    shared_hot = jax.vmap(lambda member_key: jax.random.randint(member_key, (), 0, EXPERTS, dtype=jnp.int32))(group_keys)
    use_shared = jnp.arange(groups_total) % 2 == 0
    block_keys = jax.random.split(jax.random.fold_in(key, 11), groups_total * N_EXPERT)
    routes = jax.vmap(block_routes)(block_keys, jnp.repeat(shared_hot, N_EXPERT), jnp.repeat(use_shared, N_EXPERT))
    return routes.reshape(N_SECTION, N_DP, N_EXPERT * TOK_DEV).astype(jnp.int32)


def shard_levels(key, shape, cuts, low, high):
    def one(dim, parts):
        heights = jax.random.uniform(jax.random.fold_in(jax.random.fold_in(key, 6), dim), (parts,), jnp.float32, low / len(cuts), high / len(cuts))
        return jnp.repeat(jnp.exp(heights), shape[dim] // parts).reshape((-1,) + (1,) * (len(shape) - dim - 1))

    level = one(*cuts[0])
    for cut in cuts[1:]:
        level = level * one(*cut)
    return level


def scatter_about(rng, shape, scale, most, cuts=(), kind=jnp.bfloat16):
    drawn = scale * jax.random.normal(rng, shape, jnp.float32)
    if cuts:
        drawn = drawn * shard_levels(rng, shape, cuts, -0.22, 0.18)
    return jnp.clip(drawn, -most, most).astype(kind)


def setup_inputs(seed: int = 0) -> dict:
    seeds = jax.random.split(jax.random.key(seed), 7)
    tok_input = scatter_about(seeds[0], (N_SECTION, N_DP, TOKENS, D), 1.0, 6.0, ((0, 16), (1, 4), (2, 16)))
    tok_grad = scatter_about(seeds[1], (N_SECTION, N_DP, TOKENS, D), 1.0, 6.0, ((0, 16), (1, 4), (2, 16)))
    combine_weight = jnp.clip(0.1 + 0.9 * jax.random.uniform(seeds[2], (N_SECTION, N_DP, TOKENS), jnp.float32) ** shard_levels(seeds[2], (N_SECTION, N_DP, TOKENS), ((0, 16), (1, 4), (2, 16)), -0.2, 0.2), 0.1, 1.0)
    route_expert = draw_route_expert(jax.random.fold_in(seeds[6], 71), 0)
    gate_up_weight = scatter_about(seeds[4], (N_SECTION, N_EXPERT, D, 2 * FD), D ** -0.5, 0.125, ((0, 16), (1, 16)))
    down_weight = scatter_about(seeds[5], (N_SECTION, N_EXPERT, FD, D), FF ** -0.5, 0.21875, ((0, 16), (1, 16)))
    return {"tok_input": tok_input, "tok_grad": tok_grad, "combine_weight": combine_weight, "route_expert": route_expert, "gate_up_weight": gate_up_weight, "down_weight": down_weight}


def place_rows(tokens, routes):
    blocks = tokens.reshape(N_EXPERT, TOK_DEV, D)
    route_blocks = routes.reshape(N_EXPERT, TOK_DEV).astype(jnp.int32)
    onehot = (route_blocks[:, :, None] == jnp.arange(EXPERTS, dtype=jnp.int32)[None, None, :]).astype(jnp.int32)
    slot_rank = jnp.sum((jnp.cumsum(onehot, axis=1) - onehot) * onehot, axis=2).astype(jnp.int32)
    slot_where = (route_blocks * CAP + slot_rank).astype(jnp.int32)
    empty = jnp.zeros((N_EXPERT, EXPERTS * CAP, D), tokens.dtype)
    filled = jax.vmap(lambda buffer, target, values: buffer.at[target].set(values))(empty, slot_where, blocks)
    by_expert = jnp.transpose(filled.reshape(N_EXPERT, EXPERTS, CAP, D), (1, 0, 2, 3))
    per_device = jnp.repeat(by_expert, 2, axis=0)
    return per_device.reshape(N_EXPERT, N_EXPERT * CAP, D), route_blocks, slot_rank


def one_member(tokens, grads, weights_tok, routes, gate_up, down_proj):
    scaled = (weights_tok[:, None] * grads.astype(jnp.float32)).astype(jnp.bfloat16)
    input_rows, route_blocks, slot_rank = place_rows(tokens, routes)
    grad_rows = place_rows(scaled, routes)[0]
    input_full = input_rows.astype(jnp.float32)
    grad_full = grad_rows.astype(jnp.float32)
    gate_up_full = gate_up.astype(jnp.float32)
    down_full = down_proj.astype(jnp.float32)
    preact = jnp.einsum("ird,idf->irf", input_full, gate_up_full)
    gate_act = preact[..., :FD]
    up_act = preact[..., FD:]
    unit_grad = jnp.einsum("ird,ifd->irf", grad_full, down_full)
    sigma = jax.nn.sigmoid(gate_act)
    act_grad = jnp.concatenate([unit_grad * up_act * sigma * (1.0 + gate_act * (1.0 - sigma)), unit_grad * gate_act * sigma], axis=2).astype(jnp.bfloat16)
    act_full = lax.optimization_barrier(act_grad).astype(jnp.float32)
    gate_part = jnp.einsum("ird,irf->idf", input_full, act_full)
    row_grad = jnp.einsum("irf,idf->ird", act_full, gate_up_full).astype(jnp.bfloat16)
    part_view = lax.optimization_barrier(row_grad).astype(jnp.float32).reshape(EXPERTS, 2, N_EXPERT, CAP, D)
    source = jnp.arange(N_EXPERT, dtype=jnp.int32)[:, None]
    picked = part_view[route_blocks, :, source, slot_rank]
    token_sum = (picked[:, :, 0] + picked[:, :, 1]).reshape(N_EXPERT * TOK_DEV, D)
    in_grad = (grads.astype(jnp.float32) + token_sum).astype(jnp.bfloat16)
    return gate_part, in_grad


def one_section(section_args):
    tokens, grads, weights_tok, routes, gate_up, down_proj = section_args
    gate_total = jnp.zeros((N_EXPERT, D, 2 * FD), jnp.float32)
    in_grads = []
    for member in range(N_DP):
        gate_part, in_grad = one_member(tokens[member], grads[member], weights_tok[member], routes[member], gate_up, down_proj)
        gate_total = gate_total + lax.optimization_barrier(gate_part.astype(jnp.bfloat16)).astype(jnp.float32)
        in_grads.append(in_grad)
    return gate_total.astype(jnp.bfloat16), jnp.stack(in_grads)


def reference(tok_input, tok_grad, combine_weight, route_expert, gate_up_weight, down_weight):
    gate_grads, in_grads = lax.map(one_section, (tok_input, tok_grad, combine_weight, route_expert, gate_up_weight, down_weight))
    upstream = jnp.concatenate([in_grads[1:], jnp.zeros_like(in_grads[:1])], axis=0)
    return gate_grads, upstream
```

```python
import jax
import jax.numpy as jnp
from jax import lax
from jax.sharding import Mesh, PartitionSpec as P


def shifted(block, axis, distance):
    devices = range(lax.axis_size(axis))
    route = [(i - distance, i) for i in devices if i - distance in devices]
    return lax.ppermute(block, axis, route)


def swapped(block):
    return lax.ppermute(block, "core", [(0, 1), (1, 0)])


def contract(left, right, left_dim, right_dim):
    return lax.dot_general(
        left, right, (((left_dim,), (right_dim,)), ((), ())), preferred_element_type=jnp.float32
    )


def shards(tok_input, tok_grad, combine_weight, route_expert, gate_up_weight, down_weight):
    token_input = tok_input[0, 0]
    token_grad = tok_grad[0, 0]
    weights_tok = combine_weight[0, 0]
    routes = route_expert[0, 0]
    gate_up = gate_up_weight[0, 0]
    down_proj = down_weight[0, 0]
    chips = lax.axis_size("x")
    tok_count, width = token_input.shape
    cap_rows = 9 * tok_count // (8 * chips)
    half_units = down_proj.shape[0]
    onehot = (routes[:, None] == jnp.arange(chips, dtype=jnp.int32)[None, :]).astype(jnp.int32)
    slot_rank = jnp.sum((jnp.cumsum(onehot, axis=0) - onehot) * onehot, axis=1)
    slot_ids = jnp.arange(chips * cap_rows, dtype=jnp.int32)
    placer = (
        (slot_ids[:, None] // cap_rows == routes[None, :])
        & (slot_ids[:, None] % cap_rows == slot_rank[None, :])
    ).astype(jnp.bfloat16)
    scaled = (weights_tok[:, None] * token_grad.astype(jnp.float32)).astype(jnp.bfloat16)
    both = jnp.concatenate([token_input, scaled], axis=1)
    send = jnp.dot(placer, both, preferred_element_type=jnp.float32).astype(jnp.bfloat16)
    mine = lax.all_to_all(send, "x", split_axis=0, concat_axis=0, tiled=True)
    other = swapped(mine)
    rows = jnp.concatenate([mine, other], axis=0)
    input_rows = rows[:, :width]
    grad_rows = rows[:, width:]
    preact = jnp.dot(input_rows, gate_up, preferred_element_type=jnp.float32)
    gate_act = preact[:, :half_units]
    up_act = preact[:, half_units:]
    unit_grad = contract(grad_rows, down_proj, 1, 1)
    sigma = jax.nn.sigmoid(gate_act)
    act_grad = jnp.concatenate(
        [
            unit_grad * up_act * sigma * (1.0 + gate_act * (1.0 - sigma)),
            unit_grad * gate_act * sigma,
        ],
        axis=1,
    ).astype(jnp.bfloat16)
    row_grad = contract(act_grad, gate_up, 1, 1).astype(jnp.bfloat16)
    local_rows = chips * cap_rows
    partner_part = swapped(row_grad[local_rows:])
    paired = (row_grad[:local_rows].astype(jnp.float32) + partner_part.astype(jnp.float32)).astype(
        jnp.bfloat16
    )
    returned = lax.all_to_all(paired, "x", split_axis=0, concat_axis=0, tiled=True)
    token_sum = contract(placer, returned, 0, 0)
    in_grad = (token_grad.astype(jnp.float32) + token_sum).astype(jnp.bfloat16)
    upstream = shifted(in_grad, "section", -1)
    gate_part = contract(input_rows, act_grad, 0, 0)
    gate_sum = lax.psum_scatter(
        gate_part.astype(jnp.bfloat16), "dp", scatter_dimension=0, tiled=True
    )
    return (gate_sum[None, None], upstream[None, None])


def solution(mesh):
    experts = mesh.shape["expert"]
    names = tuple(mesh.axis_names)
    sizes = []
    split_names = []
    for name in names:
        if name == "expert":
            sizes += [experts // 2, 2]
            split_names += ["x", "core"]
        else:
            sizes.append(mesh.shape[name])
            split_names.append(name)
    split = Mesh(mesh.devices.reshape(sizes), tuple(split_names))
    expert = ("x", "core")
    placed = (
        P("section", "dp", expert, None),
        P("section", "dp", expert, None),
        P("section", "dp", expert),
        P("section", "dp", expert),
        P("section", expert, None, None),
        P("section", expert, None, None),
    )
    return jax.shard_map(
        shards,
        mesh=split,
        in_specs=placed,
        out_specs=(P("section", expert, "dp", None), P("section", "dp", expert, None)),
        check_vma=False,
    )
```

```python
import jax
import jax.numpy as jnp
from jax import lax
from jax.sharding import Mesh, PartitionSpec as P


def shifted(block, axis, distance):
    devices = range(lax.axis_size(axis))
    route = [(i - distance, i) for i in devices if i - distance in devices]
    return lax.ppermute(block, axis, route)


def swapped(block):
    return lax.ppermute(block, "core", [(0, 1), (1, 0)])


def contract(left, right, left_dim, right_dim):
    return lax.dot_general(
        left, right, (((left_dim,), (right_dim,)), ((), ())), preferred_element_type=jnp.float32
    )


def make_placer(routes, chips, cap_rows):
    onehot = (routes[:, None] == jnp.arange(chips, dtype=jnp.int32)[None, :]).astype(jnp.int32)
    slot_rank = jnp.sum((jnp.cumsum(onehot, axis=0) - onehot) * onehot, axis=1)
    slot_ids = jnp.arange(chips * cap_rows, dtype=jnp.int32)
    return (
        (slot_ids[:, None] // cap_rows == routes[None, :])
        & (slot_ids[:, None] % cap_rows == slot_rank[None, :])
    ).astype(jnp.bfloat16)


def expert_half(rows, gate_up, down_proj, width, half_units):
    input_rows = rows[:, :width]
    grad_rows = rows[:, width:]
    preact = jnp.dot(input_rows, gate_up, preferred_element_type=jnp.float32)
    gate_act = preact[:, :half_units]
    up_act = preact[:, half_units:]
    unit_grad = contract(grad_rows, down_proj, 1, 1)
    sigma = jax.nn.sigmoid(gate_act)
    act_grad = jnp.concatenate(
        [
            unit_grad * up_act * sigma * (1.0 + gate_act * (1.0 - sigma)),
            unit_grad * gate_act * sigma,
        ],
        axis=1,
    ).astype(jnp.bfloat16)
    row_grad = contract(act_grad, gate_up, 1, 1).astype(jnp.bfloat16)
    gate_part = contract(input_rows, act_grad, 0, 0)
    return row_grad, gate_part


def shards(tok_input, tok_grad, combine_weight, route_expert, gate_up_weight, down_weight):
    token_input = tok_input[0, 0]
    token_grad = tok_grad[0, 0]
    weights_tok = combine_weight[0, 0]
    routes = route_expert[0, 0]
    gate_up = gate_up_weight[0, 0]
    down_proj = down_weight[0, 0]
    chips = lax.axis_size("x")
    sections = lax.axis_size("section")
    tok_count, width = token_input.shape
    cap_rows = 9 * tok_count // (8 * chips)
    half_units = down_proj.shape[0]
    next_grad = shifted(token_grad, "section", -1)
    next_routes = shifted(routes, "section", -1)
    placer = make_placer(routes, chips, cap_rows)
    scaled = (weights_tok[:, None] * token_grad.astype(jnp.float32)).astype(jnp.bfloat16)
    both = jnp.concatenate([token_input, scaled], axis=1)
    send = jnp.dot(placer, both, preferred_element_type=jnp.float32).astype(jnp.bfloat16)
    mine = lax.all_to_all(send, "x", split_axis=0, concat_axis=0, tiled=True)
    other = swapped(mine)
    grad_mine, gate_mine = expert_half(mine, gate_up, down_proj, width, half_units)
    grad_other, gate_other = expert_half(other, gate_up, down_proj, width, half_units)
    gate_sum = lax.psum_scatter(
        (gate_mine + gate_other).astype(jnp.bfloat16), "dp", scatter_dimension=0, tiled=True
    )
    partner_part = swapped(grad_other)
    paired = (grad_mine.astype(jnp.float32) + partner_part.astype(jnp.float32)).astype(jnp.bfloat16)
    paired = paired.reshape(chips, cap_rows, width)
    here = lax.axis_index("x")
    received = []
    for shift in range(chips):
        block = lax.dynamic_index_in_dim(paired, (here + shift) % chips, 0, keepdims=False)
        route = [
            (x * sections + s, ((x + shift) % chips) * sections + s - 1)
            for x in range(chips)
            for s in range(1, sections)
        ]
        received.append(lax.ppermute(block, ("x", "section"), route))
    returned = jnp.stack(received)
    next_placer = make_placer(next_routes, chips, cap_rows).reshape(chips, cap_rows, tok_count)
    order = (here - jnp.arange(chips, dtype=jnp.int32)) % chips
    placer_by_shift = jnp.take(next_placer, order, axis=0)
    token_sum = lax.dot_general(
        placer_by_shift, returned, (((0, 1), (0, 1)), ((), ())), preferred_element_type=jnp.float32
    )
    upstream = (next_grad.astype(jnp.float32) + token_sum).astype(jnp.bfloat16)
    return (gate_sum[None, None], upstream[None, None])


def solution(mesh):
    experts = mesh.shape["expert"]
    sizes = []
    split_names = []
    for name in mesh.axis_names:
        if name == "expert":
            sizes += [experts // 2, 2]
            split_names += ["x", "core"]
        else:
            sizes.append(mesh.shape[name])
            split_names.append(name)
    split = Mesh(mesh.devices.reshape(sizes), tuple(split_names))
    expert = ("x", "core")
    placed = (
        P("section", "dp", expert, None),
        P("section", "dp", expert, None),
        P("section", "dp", expert),
        P("section", "dp", expert),
        P("section", expert, None, None),
        P("section", expert, None, None),
    )
    return jax.shard_map(
        shards,
        mesh=split,
        in_specs=placed,
        out_specs=(P("section", expert, "dp", None), P("section", "dp", expert, None)),
        check_vma=False,
    )
```

```python
import jax
import jax.numpy as jnp
from jax import lax
from jax.sharding import Mesh, PartitionSpec as P


def shifted(block, axis, distance):
    devices = range(lax.axis_size(axis))
    route = [(i - distance, i) for i in devices if i - distance in devices]
    return lax.ppermute(block, axis, route)


def swapped(block):
    return lax.ppermute(block, "core", [(0, 1), (1, 0)])


def contract(left, right, left_dim, right_dim):
    return lax.dot_general(
        left, right, (((left_dim,), (right_dim,)), ((), ())), preferred_element_type=jnp.float32
    )


def make_placer(routes, chips, cap_rows):
    onehot = (routes[:, None] == jnp.arange(chips, dtype=jnp.int32)[None, :]).astype(jnp.int32)
    slot_rank = jnp.sum((jnp.cumsum(onehot, axis=0) - onehot) * onehot, axis=1)
    slot_ids = jnp.arange(chips * cap_rows, dtype=jnp.int32)
    return (
        (slot_ids[:, None] // cap_rows == routes[None, :])
        & (slot_ids[:, None] % cap_rows == slot_rank[None, :])
    ).astype(jnp.bfloat16)


def expert_half(rows, gate_up, down_proj, width, half_units):
    input_rows = rows[:, :width]
    grad_rows = rows[:, width:]
    preact = jnp.dot(input_rows, gate_up, preferred_element_type=jnp.float32)
    gate_act = preact[:, :half_units]
    up_act = preact[:, half_units:]
    unit_grad = contract(grad_rows, down_proj, 1, 1)
    sigma = jax.nn.sigmoid(gate_act)
    act_grad = jnp.concatenate(
        [
            unit_grad * up_act * sigma * (1.0 + gate_act * (1.0 - sigma)),
            unit_grad * gate_act * sigma,
        ],
        axis=1,
    ).astype(jnp.bfloat16)
    row_grad = contract(act_grad, gate_up, 1, 1).astype(jnp.bfloat16)
    gate_part = contract(input_rows, act_grad, 0, 0)
    return row_grad, gate_part


def ring_scatter(part, axis):
    count = lax.axis_size(axis)
    here = lax.axis_index(axis)
    rows, cols = part.shape
    blocks = part.reshape(count, rows // count, cols)
    ahead = blocks[:, :, : cols // 2]
    behind = blocks[:, :, cols // 2 :]
    right = [(j, (j + 1) % count) for j in range(count)]
    left = [(j, (j - 1) % count) for j in range(count)]

    def pick(stack, index):
        return lax.dynamic_index_in_dim(stack, index % count, 0, keepdims=False)

    acc_ahead = pick(ahead, here - 1)
    acc_behind = pick(behind, here + 1)
    for step in range(count - 1):
        got_ahead = lax.ppermute(acc_ahead, axis, right)
        got_behind = lax.ppermute(acc_behind, axis, left)
        acc_ahead = got_ahead.astype(jnp.float32) + pick(ahead, here - step - 2).astype(jnp.float32)
        acc_behind = got_behind.astype(jnp.float32) + pick(behind, here + step + 2).astype(jnp.float32)
        if step < count - 2:
            acc_ahead = acc_ahead.astype(jnp.bfloat16)
            acc_behind = acc_behind.astype(jnp.bfloat16)
    return jnp.concatenate([acc_ahead, acc_behind], axis=1).astype(jnp.bfloat16)


def shards(tok_input, tok_grad, combine_weight, route_expert, gate_up_weight, down_weight):
    token_input = tok_input[0, 0]
    token_grad = tok_grad[0, 0]
    weights_tok = combine_weight[0, 0]
    routes = route_expert[0, 0]
    gate_up = gate_up_weight[0, 0]
    down_proj = down_weight[0, 0]
    chips = lax.axis_size("x")
    sections = lax.axis_size("section")
    tok_count, width = token_input.shape
    cap_rows = 9 * tok_count // (8 * chips)
    half_units = down_proj.shape[0]
    next_grad = shifted(token_grad, "section", -1)
    next_routes = shifted(routes, "section", -1)
    placer = make_placer(routes, chips, cap_rows)
    scaled = (weights_tok[:, None] * token_grad.astype(jnp.float32)).astype(jnp.bfloat16)
    both = jnp.concatenate([token_input, scaled], axis=1)
    send = jnp.dot(placer, both, preferred_element_type=jnp.float32).astype(jnp.bfloat16)
    mine = lax.all_to_all(send, "x", split_axis=0, concat_axis=0, tiled=True)
    other = swapped(mine)
    grad_mine, gate_mine = expert_half(mine, gate_up, down_proj, width, half_units)
    grad_other, gate_other = expert_half(other, gate_up, down_proj, width, half_units)
    gate_sum = ring_scatter((gate_mine + gate_other).astype(jnp.bfloat16), "dp")
    partner_part = swapped(grad_other)
    paired = (grad_mine.astype(jnp.float32) + partner_part.astype(jnp.float32)).astype(jnp.bfloat16)
    paired = paired.reshape(chips, cap_rows, width)
    here = lax.axis_index("x")
    received = []
    for shift in range(chips):
        block = lax.dynamic_index_in_dim(paired, (here + shift) % chips, 0, keepdims=False)
        route = [
            (x * sections + s, ((x + shift) % chips) * sections + s - 1)
            for x in range(chips)
            for s in range(1, sections)
        ]
        received.append(lax.ppermute(block, ("x", "section"), route))
    returned = jnp.stack(received)
    next_placer = make_placer(next_routes, chips, cap_rows).reshape(chips, cap_rows, tok_count)
    order = (here - jnp.arange(chips, dtype=jnp.int32)) % chips
    placer_by_shift = jnp.take(next_placer, order, axis=0)
    token_sum = lax.dot_general(
        placer_by_shift, returned, (((0, 1), (0, 1)), ((), ())), preferred_element_type=jnp.float32
    )
    upstream = (next_grad.astype(jnp.float32) + token_sum).astype(jnp.bfloat16)
    return (gate_sum[None, None], upstream[None, None])


def solution(mesh):
    experts = mesh.shape["expert"]
    sizes = []
    split_names = []
    for name in mesh.axis_names:
        if name == "expert":
            sizes += [experts // 2, 2]
            split_names += ["x", "core"]
        else:
            sizes.append(mesh.shape[name])
            split_names.append(name)
    split = Mesh(mesh.devices.reshape(sizes), tuple(split_names))
    expert = ("x", "core")
    placed = (
        P("section", "dp", expert, None),
        P("section", "dp", expert, None),
        P("section", "dp", expert),
        P("section", "dp", expert),
        P("section", expert, None, None),
        P("section", expert, None, None),
    )
    return jax.shard_map(
        shards,
        mesh=split,
        in_specs=placed,
        out_specs=(P("section", expert, "dp", None), P("section", "dp", expert, None)),
        check_vma=False,
    )
```

```python
import jax
import jax.numpy as jnp
from jax import lax
from jax.sharding import Mesh, PartitionSpec as P


def shifted(block, axis, distance):
    devices = range(lax.axis_size(axis))
    route = [(i - distance, i) for i in devices if i - distance in devices]
    return lax.ppermute(block, axis, route)


def swapped(block):
    return lax.ppermute(block, "core", [(0, 1), (1, 0)])


def contract(left, right, left_dim, right_dim):
    return lax.dot_general(
        left, right, (((left_dim,), (right_dim,)), ((), ())), preferred_element_type=jnp.float32
    )


def make_placer(routes, chips, cap_rows):
    onehot = (routes[:, None] == jnp.arange(chips, dtype=jnp.int32)[None, :]).astype(jnp.int32)
    slot_rank = jnp.sum((jnp.cumsum(onehot, axis=0) - onehot) * onehot, axis=1)
    slot_ids = jnp.arange(chips * cap_rows, dtype=jnp.int32)
    return (
        (slot_ids[:, None] // cap_rows == routes[None, :])
        & (slot_ids[:, None] % cap_rows == slot_rank[None, :])
    ).astype(jnp.bfloat16)


def expert_half(rows, gate_up, down_proj, width, half_units):
    input_rows = rows[:, :width]
    grad_rows = rows[:, width:]
    preact = jnp.dot(input_rows, gate_up, preferred_element_type=jnp.float32)
    gate_act = preact[:, :half_units]
    up_act = preact[:, half_units:]
    unit_grad = contract(grad_rows, down_proj, 1, 1)
    sigma = jax.nn.sigmoid(gate_act)
    act_grad = jnp.concatenate(
        [
            unit_grad * up_act * sigma * (1.0 + gate_act * (1.0 - sigma)),
            unit_grad * gate_act * sigma,
        ],
        axis=1,
    ).astype(jnp.bfloat16)
    row_grad = contract(act_grad, gate_up, 1, 1).astype(jnp.bfloat16)
    gate_part = contract(input_rows, act_grad, 0, 0)
    return row_grad, gate_part


def shards(tok_input, tok_grad, combine_weight, route_expert, gate_up_weight, down_weight):
    token_input = tok_input[0, 0]
    token_grad = tok_grad[0, 0]
    weights_tok = combine_weight[0, 0]
    routes = route_expert[0, 0]
    gate_up = gate_up_weight[0, 0]
    down_proj = down_weight[0, 0]
    chips = lax.axis_size("x")
    sections = lax.axis_size("section")
    tok_count, width = token_input.shape
    cap_rows = 9 * tok_count // (8 * chips)
    half_units = down_proj.shape[0]
    next_grad = shifted(token_grad, "section", -1)
    next_routes = shifted(routes, "section", -1)
    placer = make_placer(routes, chips, cap_rows)
    scaled = (weights_tok[:, None] * token_grad.astype(jnp.float32)).astype(jnp.bfloat16)
    both = jnp.concatenate([token_input, scaled], axis=1)
    send = jnp.dot(placer, both, preferred_element_type=jnp.float32).astype(jnp.bfloat16)
    mine = lax.all_to_all(send, "x", split_axis=0, concat_axis=0, tiled=True)
    mine, next_grad, next_routes = lax.optimization_barrier((mine, next_grad, next_routes))
    other = swapped(mine)
    grad_mine, gate_mine = expert_half(mine, gate_up, down_proj, width, half_units)
    grad_other, gate_other = expert_half(other, gate_up, down_proj, width, half_units)
    gate_sum = lax.psum_scatter(
        (gate_mine + gate_other).astype(jnp.bfloat16), "dp", scatter_dimension=0, tiled=True
    )
    partner_part = swapped(grad_other)
    paired = (grad_mine.astype(jnp.float32) + partner_part.astype(jnp.float32)).astype(jnp.bfloat16)
    paired = paired.reshape(chips, cap_rows, width)
    here = lax.axis_index("x")
    received = []
    for shift in range(chips):
        block = lax.dynamic_index_in_dim(paired, (here + shift) % chips, 0, keepdims=False)
        route = [
            (x * sections + s, ((x + shift) % chips) * sections + s - 1)
            for x in range(chips)
            for s in range(1, sections)
        ]
        received.append(lax.ppermute(block, ("x", "section"), route))
    returned = jnp.stack(received)
    next_placer = make_placer(next_routes, chips, cap_rows).reshape(chips, cap_rows, tok_count)
    order = (here - jnp.arange(chips, dtype=jnp.int32)) % chips
    placer_by_shift = jnp.take(next_placer, order, axis=0)
    token_sum = lax.dot_general(
        placer_by_shift, returned, (((0, 1), (0, 1)), ((), ())), preferred_element_type=jnp.float32
    )
    upstream = (next_grad.astype(jnp.float32) + token_sum).astype(jnp.bfloat16)
    return (gate_sum[None, None], upstream[None, None])


def solution(mesh):
    experts = mesh.shape["expert"]
    sizes = []
    split_names = []
    for name in mesh.axis_names:
        if name == "expert":
            sizes += [experts // 2, 2]
            split_names += ["x", "core"]
        else:
            sizes.append(mesh.shape[name])
            split_names.append(name)
    split = Mesh(mesh.devices.reshape(sizes), tuple(split_names))
    expert = ("x", "core")
    placed = (
        P("section", "dp", expert, None),
        P("section", "dp", expert, None),
        P("section", "dp", expert),
        P("section", "dp", expert),
        P("section", expert, None, None),
        P("section", expert, None, None),
    )
    return jax.shard_map(
        shards,
        mesh=split,
        in_specs=placed,
        out_specs=(P("section", expert, "dp", None), P("section", "dp", expert, None)),
        check_vma=False,
    )
```

```python
import jax
import jax.numpy as jnp
from jax import lax
from jax.sharding import Mesh, PartitionSpec as P


def shifted(block, axis, distance):
    devices = range(lax.axis_size(axis))
    route = [(i - distance, i) for i in devices if i - distance in devices]
    return lax.ppermute(block, axis, route)


def swapped(block):
    return lax.ppermute(block, "core", [(0, 1), (1, 0)])


def contract(left, right, left_dim, right_dim):
    return lax.dot_general(
        left, right, (((left_dim,), (right_dim,)), ((), ())), preferred_element_type=jnp.float32
    )


def shards(tok_input, tok_grad, combine_weight, route_expert, gate_up_weight, down_weight):
    token_input = tok_input[0, 0]
    token_grad = tok_grad[0, 0]
    weights_tok = combine_weight[0, 0]
    routes = route_expert[0, 0]
    gate_up = gate_up_weight[0, 0]
    down_proj = down_weight[0, 0]
    chips = lax.axis_size("x")
    tok_count, width = token_input.shape
    cap_rows = 9 * tok_count // (8 * chips)
    half_units = down_proj.shape[0]
    onehot = (routes[:, None] == jnp.arange(chips, dtype=jnp.int32)[None, :]).astype(jnp.int32)
    slot_rank = jnp.sum((jnp.cumsum(onehot, axis=0) - onehot) * onehot, axis=1)
    slot_ids = jnp.arange(chips * cap_rows, dtype=jnp.int32)
    placer = (
        (slot_ids[:, None] // cap_rows == routes[None, :])
        & (slot_ids[:, None] % cap_rows == slot_rank[None, :])
    ).astype(jnp.bfloat16)
    scaled = (weights_tok[:, None] * token_grad.astype(jnp.float32)).astype(jnp.bfloat16)
    both = jnp.concatenate([token_input, scaled], axis=1)
    send = jnp.dot(placer, both, preferred_element_type=jnp.float32).astype(jnp.bfloat16)
    mine = lax.all_to_all(send, "x", split_axis=0, concat_axis=0, tiled=True)
    other = swapped(mine)
    rows = jnp.concatenate([mine, other], axis=0)
    input_rows = rows[:, :width]
    grad_rows = rows[:, width:]
    preact = jnp.dot(input_rows, gate_up, preferred_element_type=jnp.float32)
    gate_act = preact[:, :half_units]
    up_act = preact[:, half_units:]
    unit_grad = contract(grad_rows, down_proj, 1, 1)
    sigma = jax.nn.sigmoid(gate_act)
    act_grad = jnp.concatenate(
        [
            unit_grad * up_act * sigma * (1.0 + gate_act * (1.0 - sigma)),
            unit_grad * gate_act * sigma,
        ],
        axis=1,
    ).astype(jnp.bfloat16)
    row_grad = contract(act_grad, gate_up, 1, 1).astype(jnp.bfloat16)
    local_rows = chips * cap_rows
    partner_part = swapped(row_grad[local_rows:])
    paired = (row_grad[:local_rows].astype(jnp.float32) + partner_part.astype(jnp.float32)).astype(
        jnp.bfloat16
    )
    returned = lax.all_to_all(paired, "x", split_axis=0, concat_axis=0, tiled=True)
    token_sum = contract(placer, returned, 0, 0)
    in_grad = (token_grad.astype(jnp.float32) + token_sum).astype(jnp.bfloat16)
    gate_part = contract(input_rows, act_grad, 0, 0)
    gate_sum = lax.psum_scatter(
        gate_part.astype(jnp.bfloat16), "dp", scatter_dimension=0, tiled=True
    )
    gate_sum, in_grad = lax.optimization_barrier((gate_sum, in_grad))
    upstream = shifted(in_grad, "section", -1)
    return (gate_sum[None, None], upstream[None, None])


def solution(mesh):
    experts = mesh.shape["expert"]
    names = tuple(mesh.axis_names)
    sizes = []
    split_names = []
    for name in names:
        if name == "expert":
            sizes += [experts // 2, 2]
            split_names += ["x", "core"]
        else:
            sizes.append(mesh.shape[name])
            split_names.append(name)
    split = Mesh(mesh.devices.reshape(sizes), tuple(split_names))
    expert = ("x", "core")
    placed = (
        P("section", "dp", expert, None),
        P("section", "dp", expert, None),
        P("section", "dp", expert),
        P("section", "dp", expert),
        P("section", expert, None, None),
        P("section", expert, None, None),
    )
    return jax.shard_map(
        shards,
        mesh=split,
        in_specs=placed,
        out_specs=(P("section", expert, "dp", None), P("section", "dp", expert, None)),
        check_vma=False,
    )
```

```python
import jax
import jax.numpy as jnp
from jax import lax
from jax.sharding import Mesh, PartitionSpec as P


def shifted(block, axis, distance):
    devices = range(lax.axis_size(axis))
    route = [(i - distance, i) for i in devices if i - distance in devices]
    return lax.ppermute(block, axis, route)


def swapped(block):
    return lax.ppermute(block, "core", [(0, 1), (1, 0)])


def exchanged(rows, parts):
    lanes = 128
    count, width = rows.shape
    blocks = rows.reshape(parts, count * width // (parts * lanes), lanes)
    moved = lax.all_to_all(blocks, "x", split_axis=0, concat_axis=0, tiled=True)
    return moved.reshape(count, width)


def contract(left, right, left_dim, right_dim):
    return lax.dot_general(
        left, right, (((left_dim,), (right_dim,)), ((), ())), preferred_element_type=jnp.float32
    )


def shards(tok_input, tok_grad, combine_weight, route_expert, gate_up_weight, down_weight):
    token_input = tok_input[0, 0]
    token_grad = tok_grad[0, 0]
    weights_tok = combine_weight[0, 0]
    routes = route_expert[0, 0]
    gate_up = gate_up_weight[0, 0]
    down_proj = down_weight[0, 0]
    chips = lax.axis_size("x")
    tok_count, width = token_input.shape
    cap_rows = 9 * tok_count // (8 * chips)
    half_units = down_proj.shape[0]
    onehot = (routes[:, None] == jnp.arange(chips, dtype=jnp.int32)[None, :]).astype(jnp.int32)
    slot_rank = jnp.sum((jnp.cumsum(onehot, axis=0) - onehot) * onehot, axis=1)
    slot_ids = jnp.arange(chips * cap_rows, dtype=jnp.int32)
    placer = (
        (slot_ids[:, None] // cap_rows == routes[None, :])
        & (slot_ids[:, None] % cap_rows == slot_rank[None, :])
    ).astype(jnp.bfloat16)
    scaled = (weights_tok[:, None] * token_grad.astype(jnp.float32)).astype(jnp.bfloat16)
    both = jnp.concatenate([token_input, scaled], axis=1)
    send = jnp.dot(placer, both, preferred_element_type=jnp.float32).astype(jnp.bfloat16)
    mine = exchanged(send, chips)
    other = swapped(mine)
    rows = jnp.concatenate([mine, other], axis=0)
    input_rows = rows[:, :width]
    grad_rows = rows[:, width:]
    preact = jnp.dot(input_rows, gate_up, preferred_element_type=jnp.float32)
    gate_act = preact[:, :half_units]
    up_act = preact[:, half_units:]
    unit_grad = contract(grad_rows, down_proj, 1, 1)
    sigma = jax.nn.sigmoid(gate_act)
    act_grad = jnp.concatenate(
        [
            unit_grad * up_act * sigma * (1.0 + gate_act * (1.0 - sigma)),
            unit_grad * gate_act * sigma,
        ],
        axis=1,
    ).astype(jnp.bfloat16)
    row_grad = contract(act_grad, gate_up, 1, 1).astype(jnp.bfloat16)
    local_rows = chips * cap_rows
    partner_part = swapped(row_grad[local_rows:])
    paired = (row_grad[:local_rows].astype(jnp.float32) + partner_part.astype(jnp.float32)).astype(
        jnp.bfloat16
    )
    returned = exchanged(paired, chips)
    token_sum = contract(placer, returned, 0, 0)
    in_grad = (token_grad.astype(jnp.float32) + token_sum).astype(jnp.bfloat16)
    upstream = shifted(in_grad, "section", -1)
    gate_part = contract(input_rows, act_grad, 0, 0)
    gate_sum = lax.psum_scatter(
        gate_part.astype(jnp.bfloat16), "dp", scatter_dimension=0, tiled=True
    )
    return (gate_sum[None, None], upstream[None, None])


def solution(mesh):
    experts = mesh.shape["expert"]
    names = tuple(mesh.axis_names)
    sizes = []
    split_names = []
    for name in names:
        if name == "expert":
            sizes += [experts // 2, 2]
            split_names += ["x", "core"]
        else:
            sizes.append(mesh.shape[name])
            split_names.append(name)
    split = Mesh(mesh.devices.reshape(sizes), tuple(split_names))
    expert = ("x", "core")
    placed = (
        P("section", "dp", expert, None),
        P("section", "dp", expert, None),
        P("section", "dp", expert),
        P("section", "dp", expert),
        P("section", expert, None, None),
        P("section", expert, None, None),
    )
    return jax.shard_map(
        shards,
        mesh=split,
        in_specs=placed,
        out_specs=(P("section", expert, "dp", None), P("section", "dp", expert, None)),
        check_vma=False,
    )
```

```python
import jax
import jax.numpy as jnp
from jax import lax
from jax.sharding import Mesh, PartitionSpec as P


def shifted(block, axis, distance):
    devices = range(lax.axis_size(axis))
    route = [(i - distance, i) for i in devices if i - distance in devices]
    return lax.ppermute(block, axis, route)


def swapped(block):
    return lax.ppermute(block, "core", [(0, 1), (1, 0)])


def exchanged(rows, parts):
    lanes = 128
    count, width = rows.shape
    blocks = rows.reshape(parts, count * width // (parts * lanes), lanes)
    moved = lax.all_to_all(blocks, "x", split_axis=0, concat_axis=0, tiled=True)
    return moved.reshape(count, width)


def contract(left, right, left_dim, right_dim):
    return lax.dot_general(
        left, right, (((left_dim,), (right_dim,)), ((), ())), preferred_element_type=jnp.float32
    )


def shards(tok_input, tok_grad, combine_weight, route_expert, gate_up_weight, down_weight):
    token_input = tok_input[0, 0]
    token_grad = tok_grad[0, 0]
    weights_tok = combine_weight[0, 0]
    routes = route_expert[0, 0]
    gate_up = gate_up_weight[0, 0]
    down_proj = down_weight[0, 0]
    chips = lax.axis_size("x")
    tok_count, width = token_input.shape
    cap_rows = 9 * tok_count // (8 * chips)
    half_units = down_proj.shape[0]
    onehot = (routes[:, None] == jnp.arange(chips, dtype=jnp.int32)[None, :]).astype(jnp.int32)
    slot_rank = jnp.sum((jnp.cumsum(onehot, axis=0) - onehot) * onehot, axis=1)
    slot_ids = jnp.arange(chips * cap_rows, dtype=jnp.int32)
    placer = (
        (slot_ids[:, None] // cap_rows == routes[None, :])
        & (slot_ids[:, None] % cap_rows == slot_rank[None, :])
    ).astype(jnp.bfloat16)
    scaled = (weights_tok[:, None] * token_grad.astype(jnp.float32)).astype(jnp.bfloat16)
    both = jnp.concatenate([token_input, scaled], axis=1)
    send = jnp.dot(placer, both, preferred_element_type=jnp.float32).astype(jnp.bfloat16)
    mine = exchanged(send, chips)
    other = swapped(mine)
    rows = jnp.concatenate([mine, other], axis=0)
    input_rows = rows[:, :width]
    grad_rows = rows[:, width:]
    preact = jnp.dot(input_rows, gate_up, preferred_element_type=jnp.float32)
    gate_act = preact[:, :half_units]
    up_act = preact[:, half_units:]
    unit_grad = contract(grad_rows, down_proj, 1, 1)
    sigma = jax.nn.sigmoid(gate_act)
    act_grad = jnp.concatenate(
        [
            unit_grad * up_act * sigma * (1.0 + gate_act * (1.0 - sigma)),
            unit_grad * gate_act * sigma,
        ],
        axis=1,
    ).astype(jnp.bfloat16)
    row_grad = contract(act_grad, gate_up, 1, 1).astype(jnp.bfloat16)
    local_rows = chips * cap_rows
    partner_part = swapped(row_grad[local_rows:])
    paired = (row_grad[:local_rows].astype(jnp.float32) + partner_part.astype(jnp.float32)).astype(
        jnp.bfloat16
    )
    returned = exchanged(paired, chips)
    token_sum = contract(placer, returned, 0, 0)
    in_grad = (token_grad.astype(jnp.float32) + token_sum).astype(jnp.bfloat16)
    upstream = shifted(in_grad, "section", -1)
    gate_part = contract(input_rows, act_grad, 0, 0)
    gate_total = gate_part.astype(jnp.bfloat16)
    groups = lax.axis_size("dp")
    direct_cols = 256
    ring_cols = gate_total.shape[1] - direct_cols
    gate_ring = lax.psum_scatter(gate_total[:, :ring_cols], "dp", scatter_dimension=0, tiled=True)
    direct = gate_total[:, ring_cols:].reshape(groups, gate_total.shape[0] // groups, direct_cols)
    direct = lax.all_to_all(direct, "dp", split_axis=0, concat_axis=0, tiled=True)
    gate_direct = jnp.sum(direct.astype(jnp.float32), axis=0).astype(jnp.bfloat16)
    gate_sum = jnp.concatenate([gate_ring, gate_direct], axis=1)
    return (gate_sum[None, None], upstream[None, None])


def solution(mesh):
    experts = mesh.shape["expert"]
    names = tuple(mesh.axis_names)
    sizes = []
    split_names = []
    for name in names:
        if name == "expert":
            sizes += [experts // 2, 2]
            split_names += ["x", "core"]
        else:
            sizes.append(mesh.shape[name])
            split_names.append(name)
    split = Mesh(mesh.devices.reshape(sizes), tuple(split_names))
    expert = ("x", "core")
    placed = (
        P("section", "dp", expert, None),
        P("section", "dp", expert, None),
        P("section", "dp", expert),
        P("section", "dp", expert),
        P("section", expert, None, None),
        P("section", expert, None, None),
    )
    return jax.shard_map(
        shards,
        mesh=split,
        in_specs=placed,
        out_specs=(P("section", expert, "dp", None), P("section", "dp", expert, None)),
        check_vma=False,
    )
```

```python
import jax
import jax.numpy as jnp
from jax import lax
from jax.sharding import Mesh, PartitionSpec as P


def shifted(block, axis, distance):
    devices = range(lax.axis_size(axis))
    route = [(i - distance, i) for i in devices if i - distance in devices]
    return lax.ppermute(block, axis, route)


def swapped(block):
    return lax.ppermute(block, "core", [(0, 1), (1, 0)])


def exchanged(rows, parts):
    lanes = 128
    count, width = rows.shape
    blocks = rows.reshape(parts, count * width // (parts * lanes), lanes)
    moved = lax.all_to_all(blocks, "x", split_axis=0, concat_axis=0, tiled=True)
    return moved.reshape(count, width)


def contract(left, right, left_dim, right_dim):
    return lax.dot_general(
        left, right, (((left_dim,), (right_dim,)), ((), ())), preferred_element_type=jnp.float32
    )


def shards(tok_input, tok_grad, combine_weight, route_expert, gate_up_weight, down_weight):
    token_input = tok_input[0, 0]
    token_grad = tok_grad[0, 0]
    weights_tok = combine_weight[0, 0]
    routes = route_expert[0, 0]
    gate_up = gate_up_weight[0, 0]
    down_proj = down_weight[0, 0]
    chips = lax.axis_size("x")
    tok_count, width = token_input.shape
    cap_rows = 9 * tok_count // (8 * chips)
    half_units = down_proj.shape[0]
    onehot = (routes[:, None] == jnp.arange(chips, dtype=jnp.int32)[None, :]).astype(jnp.int32)
    slot_rank = jnp.sum((jnp.cumsum(onehot, axis=0) - onehot) * onehot, axis=1)
    slot_ids = jnp.arange(chips * cap_rows, dtype=jnp.int32)
    placer = (
        (slot_ids[:, None] // cap_rows == routes[None, :])
        & (slot_ids[:, None] % cap_rows == slot_rank[None, :])
    ).astype(jnp.bfloat16)
    scaled = (weights_tok[:, None] * token_grad.astype(jnp.float32)).astype(jnp.bfloat16)
    send_input = jnp.dot(placer, token_input, preferred_element_type=jnp.float32).astype(jnp.bfloat16)
    send_grad = jnp.dot(placer, scaled, preferred_element_type=jnp.float32).astype(jnp.bfloat16)
    mine_input = exchanged(send_input, chips)
    mine_grad = exchanged(send_grad, chips)
    input_rows = jnp.concatenate([mine_input, swapped(mine_input)], axis=0)
    grad_rows = jnp.concatenate([mine_grad, swapped(mine_grad)], axis=0)
    preact = jnp.dot(input_rows, gate_up, preferred_element_type=jnp.float32)
    gate_act = preact[:, :half_units]
    up_act = preact[:, half_units:]
    unit_grad = contract(grad_rows, down_proj, 1, 1)
    sigma = jax.nn.sigmoid(gate_act)
    act_grad = jnp.concatenate(
        [
            unit_grad * up_act * sigma * (1.0 + gate_act * (1.0 - sigma)),
            unit_grad * gate_act * sigma,
        ],
        axis=1,
    ).astype(jnp.bfloat16)
    row_grad = contract(act_grad, gate_up, 1, 1).astype(jnp.bfloat16)
    local_rows = chips * cap_rows
    partner_part = swapped(row_grad[local_rows:])
    paired = (row_grad[:local_rows].astype(jnp.float32) + partner_part.astype(jnp.float32)).astype(
        jnp.bfloat16
    )
    returned = exchanged(paired, chips)
    token_sum = contract(placer, returned, 0, 0)
    in_grad = (token_grad.astype(jnp.float32) + token_sum).astype(jnp.bfloat16)
    upstream = shifted(in_grad, "section", -1)
    gate_part = contract(input_rows, act_grad, 0, 0)
    gate_sum = lax.psum_scatter(
        gate_part.astype(jnp.bfloat16), "dp", scatter_dimension=0, tiled=True
    )
    return (gate_sum[None, None], upstream[None, None])


def solution(mesh):
    experts = mesh.shape["expert"]
    names = tuple(mesh.axis_names)
    sizes = []
    split_names = []
    for name in names:
        if name == "expert":
            sizes += [experts // 2, 2]
            split_names += ["x", "core"]
        else:
            sizes.append(mesh.shape[name])
            split_names.append(name)
    split = Mesh(mesh.devices.reshape(sizes), tuple(split_names))
    expert = ("x", "core")
    placed = (
        P("section", "dp", expert, None),
        P("section", "dp", expert, None),
        P("section", "dp", expert),
        P("section", "dp", expert),
        P("section", expert, None, None),
        P("section", expert, None, None),
    )
    return jax.shard_map(
        shards,
        mesh=split,
        in_specs=placed,
        out_specs=(P("section", expert, "dp", None), P("section", "dp", expert, None)),
        check_vma=False,
    )
```

```python
import jax
import jax.numpy as jnp
from jax import lax
from jax.sharding import Mesh, PartitionSpec as P


def shifted(block, axis, distance):
    devices = range(lax.axis_size(axis))
    route = [(i - distance, i) for i in devices if i - distance in devices]
    return lax.ppermute(block, axis, route)


def swapped(block):
    return lax.ppermute(block, "core", [(0, 1), (1, 0)])


def contract(left, right, left_dim, right_dim):
    return lax.dot_general(
        left, right, (((left_dim,), (right_dim,)), ((), ())), preferred_element_type=jnp.float32
    )


def make_placer(routes, chips, cap_rows):
    onehot = (routes[:, None] == jnp.arange(chips, dtype=jnp.int32)[None, :]).astype(jnp.int32)
    slot_rank = jnp.sum((jnp.cumsum(onehot, axis=0) - onehot) * onehot, axis=1)
    slot_ids = jnp.arange(chips * cap_rows, dtype=jnp.int32)
    return (
        (slot_ids[:, None] // cap_rows == routes[None, :])
        & (slot_ids[:, None] % cap_rows == slot_rank[None, :])
    ).astype(jnp.bfloat16)


def expert_half(rows, gate_up, down_proj, width, half_units):
    input_rows = rows[:, :width]
    grad_rows = rows[:, width:]
    preact = jnp.dot(input_rows, gate_up, preferred_element_type=jnp.float32)
    gate_act = preact[:, :half_units]
    up_act = preact[:, half_units:]
    unit_grad = contract(grad_rows, down_proj, 1, 1)
    sigma = jax.nn.sigmoid(gate_act)
    act_grad = jnp.concatenate(
        [
            unit_grad * up_act * sigma * (1.0 + gate_act * (1.0 - sigma)),
            unit_grad * gate_act * sigma,
        ],
        axis=1,
    ).astype(jnp.bfloat16)
    row_grad = contract(act_grad, gate_up, 1, 1).astype(jnp.bfloat16)
    gate_part = contract(input_rows, act_grad, 0, 0)
    return row_grad, gate_part


def shards(tok_input, tok_grad, combine_weight, route_expert, gate_up_weight, down_weight):
    token_input = tok_input[0, 0]
    token_grad = tok_grad[0, 0]
    weights_tok = combine_weight[0, 0]
    routes = route_expert[0, 0]
    gate_up = gate_up_weight[0, 0]
    down_proj = down_weight[0, 0]
    chips = lax.axis_size("x")
    sections = lax.axis_size("section")
    tok_count, width = token_input.shape
    cap_rows = 9 * tok_count // (8 * chips)
    half_units = down_proj.shape[0]
    next_grad = shifted(token_grad, "section", -1)
    next_routes = shifted(routes, "section", -1)
    placer = make_placer(routes, chips, cap_rows)
    scaled = (weights_tok[:, None] * token_grad.astype(jnp.float32)).astype(jnp.bfloat16)
    both = jnp.concatenate([token_input, scaled], axis=1)
    send = jnp.dot(placer, both, preferred_element_type=jnp.float32).astype(jnp.bfloat16)
    lanes = 128
    blocks = send.reshape(chips, send.size // (chips * lanes), lanes)
    mine = lax.all_to_all(blocks, "x", split_axis=0, concat_axis=0, tiled=True).reshape(send.shape)
    mine, next_grad, next_routes = lax.optimization_barrier((mine, next_grad, next_routes))
    other = swapped(mine)
    grad_mine, gate_mine = expert_half(mine, gate_up, down_proj, width, half_units)
    grad_other, gate_other = expert_half(other, gate_up, down_proj, width, half_units)
    gate_sum = lax.psum_scatter(
        (gate_mine + gate_other).astype(jnp.bfloat16), "dp", scatter_dimension=0, tiled=True
    )
    partner_part = swapped(grad_other)
    paired = (grad_mine.astype(jnp.float32) + partner_part.astype(jnp.float32)).astype(jnp.bfloat16)
    paired = paired.reshape(chips, cap_rows * width // lanes, lanes)
    here = lax.axis_index("x")
    received = []
    for shift in range(chips):
        block = lax.dynamic_index_in_dim(paired, (here + shift) % chips, 0, keepdims=False)
        route = [
            (x * sections + s, ((x + shift) % chips) * sections + s - 1)
            for x in range(chips)
            for s in range(1, sections)
        ]
        received.append(lax.ppermute(block, ("x", "section"), route))
    returned = jnp.stack(received).reshape(chips, cap_rows, width)
    next_placer = make_placer(next_routes, chips, cap_rows).reshape(chips, cap_rows, tok_count)
    order = (here - jnp.arange(chips, dtype=jnp.int32)) % chips
    placer_by_shift = jnp.take(next_placer, order, axis=0)
    token_sum = lax.dot_general(
        placer_by_shift, returned, (((0, 1), (0, 1)), ((), ())), preferred_element_type=jnp.float32
    )
    upstream = (next_grad.astype(jnp.float32) + token_sum).astype(jnp.bfloat16)
    return (gate_sum[None, None], upstream[None, None])


def solution(mesh):
    experts = mesh.shape["expert"]
    sizes = []
    split_names = []
    for name in mesh.axis_names:
        if name == "expert":
            sizes += [experts // 2, 2]
            split_names += ["x", "core"]
        else:
            sizes.append(mesh.shape[name])
            split_names.append(name)
    split = Mesh(mesh.devices.reshape(sizes), tuple(split_names))
    expert = ("x", "core")
    placed = (
        P("section", "dp", expert, None),
        P("section", "dp", expert, None),
        P("section", "dp", expert),
        P("section", "dp", expert),
        P("section", expert, None, None),
        P("section", expert, None, None),
    )
    return jax.shard_map(
        shards,
        mesh=split,
        in_specs=placed,
        out_specs=(P("section", expert, "dp", None), P("section", "dp", expert, None)),
        check_vma=False,
    )
```

```python
import jax
import jax.numpy as jnp
from jax import lax
from jax.sharding import Mesh, PartitionSpec as P


def shifted(block, axis, distance):
    devices = range(lax.axis_size(axis))
    route = [(i - distance, i) for i in devices if i - distance in devices]
    return lax.ppermute(block, axis, route)


def swapped(block):
    return lax.ppermute(block, "core", [(0, 1), (1, 0)])


def contract(left, right, left_dim, right_dim):
    return lax.dot_general(
        left, right, (((left_dim,), (right_dim,)), ((), ())), preferred_element_type=jnp.float32
    )


def make_placer(routes, chips, cap_rows):
    onehot = (routes[:, None] == jnp.arange(chips, dtype=jnp.int32)[None, :]).astype(jnp.int32)
    slot_rank = jnp.sum((jnp.cumsum(onehot, axis=0) - onehot) * onehot, axis=1)
    slot_ids = jnp.arange(chips * cap_rows, dtype=jnp.int32)
    return (
        (slot_ids[:, None] // cap_rows == routes[None, :])
        & (slot_ids[:, None] % cap_rows == slot_rank[None, :])
    ).astype(jnp.bfloat16)


def expert_half(rows, gate_up, down_proj, width, half_units):
    input_rows = rows[:, :width]
    grad_rows = rows[:, width:]
    preact = jnp.dot(input_rows, gate_up, preferred_element_type=jnp.float32)
    gate_act = preact[:, :half_units]
    up_act = preact[:, half_units:]
    unit_grad = contract(grad_rows, down_proj, 1, 1)
    sigma = jax.nn.sigmoid(gate_act)
    act_grad = jnp.concatenate(
        [
            unit_grad * up_act * sigma * (1.0 + gate_act * (1.0 - sigma)),
            unit_grad * gate_act * sigma,
        ],
        axis=1,
    ).astype(jnp.bfloat16)
    row_grad = contract(act_grad, gate_up, 1, 1).astype(jnp.bfloat16)
    gate_part = contract(input_rows, act_grad, 0, 0)
    return row_grad, gate_part


def shards(tok_input, tok_grad, combine_weight, route_expert, gate_up_weight, down_weight):
    token_input = tok_input[0, 0]
    token_grad = tok_grad[0, 0]
    weights_tok = combine_weight[0, 0]
    routes = route_expert[0, 0]
    gate_up = gate_up_weight[0, 0]
    down_proj = down_weight[0, 0]
    chips = lax.axis_size("x")
    sections = lax.axis_size("section")
    tok_count, width = token_input.shape
    cap_rows = 9 * tok_count // (8 * chips)
    half_units = down_proj.shape[0]
    next_grad = shifted(token_grad, "section", -1)
    next_routes = shifted(routes, "section", -1)
    placer = make_placer(routes, chips, cap_rows)
    scaled = (weights_tok[:, None] * token_grad.astype(jnp.float32)).astype(jnp.bfloat16)
    both = jnp.concatenate([token_input, scaled], axis=1)
    send = jnp.dot(placer, both, preferred_element_type=jnp.float32).astype(jnp.bfloat16)
    lanes = 128
    blocks = send.reshape(chips, send.size // (chips * lanes), lanes)
    arrived = lax.all_to_all(blocks, "x", split_axis=0, concat_axis=0, tiled=True)
    forwarded = swapped(arrived)
    mine = arrived.reshape(send.shape)
    mine, next_grad, next_routes = lax.optimization_barrier((mine, next_grad, next_routes))
    other = forwarded.reshape(send.shape)
    grad_mine, gate_mine = expert_half(mine, gate_up, down_proj, width, half_units)
    grad_other, gate_other = expert_half(other, gate_up, down_proj, width, half_units)
    gate_sum = lax.psum_scatter(
        (gate_mine + gate_other).astype(jnp.bfloat16), "dp", scatter_dimension=0, tiled=True
    )
    partner_part = swapped(grad_other)
    paired = (grad_mine.astype(jnp.float32) + partner_part.astype(jnp.float32)).astype(jnp.bfloat16)
    paired = paired.reshape(chips, cap_rows * width // lanes, lanes)
    here = lax.axis_index("x")
    received = []
    for shift in range(chips):
        block = lax.dynamic_index_in_dim(paired, (here + shift) % chips, 0, keepdims=False)
        route = [
            (x * sections + s, ((x + shift) % chips) * sections + s - 1)
            for x in range(chips)
            for s in range(1, sections)
        ]
        received.append(lax.ppermute(block, ("x", "section"), route))
    returned = jnp.stack(received).reshape(chips, cap_rows, width)
    next_placer = make_placer(next_routes, chips, cap_rows).reshape(chips, cap_rows, tok_count)
    order = (here - jnp.arange(chips, dtype=jnp.int32)) % chips
    placer_by_shift = jnp.take(next_placer, order, axis=0)
    token_sum = lax.dot_general(
        placer_by_shift, returned, (((0, 1), (0, 1)), ((), ())), preferred_element_type=jnp.float32
    )
    upstream = (next_grad.astype(jnp.float32) + token_sum).astype(jnp.bfloat16)
    return (gate_sum[None, None], upstream[None, None])


def solution(mesh):
    experts = mesh.shape["expert"]
    sizes = []
    split_names = []
    for name in mesh.axis_names:
        if name == "expert":
            sizes += [experts // 2, 2]
            split_names += ["x", "core"]
        else:
            sizes.append(mesh.shape[name])
            split_names.append(name)
    split = Mesh(mesh.devices.reshape(sizes), tuple(split_names))
    expert = ("x", "core")
    placed = (
        P("section", "dp", expert, None),
        P("section", "dp", expert, None),
        P("section", "dp", expert),
        P("section", "dp", expert),
        P("section", expert, None, None),
        P("section", expert, None, None),
    )
    return jax.shard_map(
        shards,
        mesh=split,
        in_specs=placed,
        out_specs=(P("section", expert, "dp", None), P("section", "dp", expert, None)),
        check_vma=False,
    )
```

```python
import jax
import jax.numpy as jnp
from jax import lax
from jax.sharding import Mesh, PartitionSpec as P


def shifted(block, axis, distance):
    devices = range(lax.axis_size(axis))
    route = [(i - distance, i) for i in devices if i - distance in devices]
    return lax.ppermute(block, axis, route)


def swapped(block):
    return lax.ppermute(block, "core", [(0, 1), (1, 0)])


def contract(left, right, left_dim, right_dim):
    return lax.dot_general(
        left, right, (((left_dim,), (right_dim,)), ((), ())), preferred_element_type=jnp.float32
    )


def make_placer(routes, chips, cap_rows):
    onehot = (routes[:, None] == jnp.arange(chips, dtype=jnp.int32)[None, :]).astype(jnp.int32)
    slot_rank = jnp.sum((jnp.cumsum(onehot, axis=0) - onehot) * onehot, axis=1)
    slot_ids = jnp.arange(chips * cap_rows, dtype=jnp.int32)
    return (
        (slot_ids[:, None] // cap_rows == routes[None, :])
        & (slot_ids[:, None] % cap_rows == slot_rank[None, :])
    ).astype(jnp.bfloat16)


def expert_half(rows, gate_up, down_proj, width, half_units):
    input_rows = rows[:, :width]
    grad_rows = rows[:, width:]
    preact = jnp.dot(input_rows, gate_up, preferred_element_type=jnp.float32)
    gate_act = preact[:, :half_units]
    up_act = preact[:, half_units:]
    unit_grad = contract(grad_rows, down_proj, 1, 1)
    sigma = jax.nn.sigmoid(gate_act)
    act_grad = jnp.concatenate(
        [
            unit_grad * up_act * sigma * (1.0 + gate_act * (1.0 - sigma)),
            unit_grad * gate_act * sigma,
        ],
        axis=1,
    ).astype(jnp.bfloat16)
    row_grad = contract(act_grad, gate_up, 1, 1).astype(jnp.bfloat16)
    return row_grad, act_grad


def shards(tok_input, tok_grad, combine_weight, route_expert, gate_up_weight, down_weight):
    token_input = tok_input[0, 0]
    token_grad = tok_grad[0, 0]
    weights_tok = combine_weight[0, 0]
    routes = route_expert[0, 0]
    gate_up = gate_up_weight[0, 0]
    down_proj = down_weight[0, 0]
    chips = lax.axis_size("x")
    sections = lax.axis_size("section")
    tok_count, width = token_input.shape
    cap_rows = 9 * tok_count // (8 * chips)
    half_units = down_proj.shape[0]
    next_grad = shifted(token_grad, "section", -1)
    next_routes = shifted(routes, "section", -1)
    placer = make_placer(routes, chips, cap_rows)
    scaled = (weights_tok[:, None] * token_grad.astype(jnp.float32)).astype(jnp.bfloat16)
    both = jnp.concatenate([token_input, scaled], axis=1)
    send = jnp.dot(placer, both, preferred_element_type=jnp.float32).astype(jnp.bfloat16)
    lanes = 128
    blocks = send.reshape(chips, send.size // (chips * lanes), lanes)
    mine = lax.all_to_all(blocks, "x", split_axis=0, concat_axis=0, tiled=True).reshape(send.shape)
    mine, next_grad, next_routes = lax.optimization_barrier((mine, next_grad, next_routes))
    other = swapped(mine)
    grad_mine, act_mine = expert_half(mine, gate_up, down_proj, width, half_units)
    grad_other, act_other = expert_half(other, gate_up, down_proj, width, half_units)
    gate_total = contract(
        jnp.concatenate([mine[:, :width], other[:, :width]], axis=0),
        jnp.concatenate([act_mine, act_other], axis=0),
        0,
        0,
    )
    gate_sum = lax.psum_scatter(
        gate_total.astype(jnp.bfloat16), "dp", scatter_dimension=0, tiled=True
    )
    partner_part = swapped(grad_other)
    paired = (grad_mine.astype(jnp.float32) + partner_part.astype(jnp.float32)).astype(jnp.bfloat16)
    paired = paired.reshape(chips, cap_rows * width // lanes, lanes)
    here = lax.axis_index("x")
    received = []
    for shift in range(chips):
        block = lax.dynamic_index_in_dim(paired, (here + shift) % chips, 0, keepdims=False)
        route = [
            (x * sections + s, ((x + shift) % chips) * sections + s - 1)
            for x in range(chips)
            for s in range(1, sections)
        ]
        received.append(lax.ppermute(block, ("x", "section"), route))
    returned = jnp.stack(received).reshape(chips, cap_rows, width)
    next_placer = make_placer(next_routes, chips, cap_rows).reshape(chips, cap_rows, tok_count)
    order = (here - jnp.arange(chips, dtype=jnp.int32)) % chips
    placer_by_shift = jnp.take(next_placer, order, axis=0)
    token_sum = lax.dot_general(
        placer_by_shift, returned, (((0, 1), (0, 1)), ((), ())), preferred_element_type=jnp.float32
    )
    upstream = (next_grad.astype(jnp.float32) + token_sum).astype(jnp.bfloat16)
    return (gate_sum[None, None], upstream[None, None])


def solution(mesh):
    experts = mesh.shape["expert"]
    sizes = []
    split_names = []
    for name in mesh.axis_names:
        if name == "expert":
            sizes += [experts // 2, 2]
            split_names += ["x", "core"]
        else:
            sizes.append(mesh.shape[name])
            split_names.append(name)
    split = Mesh(mesh.devices.reshape(sizes), tuple(split_names))
    expert = ("x", "core")
    placed = (
        P("section", "dp", expert, None),
        P("section", "dp", expert, None),
        P("section", "dp", expert),
        P("section", "dp", expert),
        P("section", expert, None, None),
        P("section", expert, None, None),
    )
    return jax.shard_map(
        shards,
        mesh=split,
        in_specs=placed,
        out_specs=(P("section", expert, "dp", None), P("section", "dp", expert, None)),
        check_vma=False,
    )
```
